128 devices in a mesh: fsdp: 32 (over x_lo, z, y), grp: 4 (over x_hi, core).
Axes of the slice: x: 4 (x_hi: 2, x_lo: 2; x = x_hi * 2 + x_lo), y: 4, z: 4, core: 2. Of those that a mesh axis runs over, the one named last changes fastest.
Arguments:
- latents: bfloat16 [8192, 512], P('fsdp'), may hold values from -6 to 6
- queries: bfloat16 [8192, 128, 128], P('fsdp', 'grp')
- grad_out: bfloat16 [8192, 128, 128], P('fsdp', 'grp'), may hold values from -6 to 6
- kv_weight: bfloat16 [4, 32, 512, 256], P('grp', 'fsdp'), may hold values from -0.25 to 0.25
- doc_ids: int32 [8192], replicated, may hold values from 0 to 3, never falling along the last dimension, each value on 1 to 4096 neighbouring positions
- block_lists: int32 [128, 4], replicated, may hold values from 0 to 127, as said below
Outputs:
- grad_queries: bfloat16 [8192, 128, 128], P('fsdp', 'grp')
- grad_latents: float32 [8192, 512], P('fsdp', 'grp')
- grad_weight: float32 [4, 32, 512, 256], P('grp', 'fsdp')
The draws below stay inside these ranges and needn't reach their ends.
Inputs may be any that keep to these rules, and one draw needn't show every extreme that they name: `block_lists`: row b belongs to query block b; its first entry is b and its 4 entries differ. Take the 4 rows of one run f (rows f * 4 to f * 4 + 3) without their first entries: for every d from 1 to 6 with f - d >= 0, exactly 2 of these entries, counted with repeats, are blocks of run f - d; all other entries are blocks of run f itself.
All inputs are finite; a program needn't handle non-finite values.
Results may differ from the reference program's by a relative error of at most 0.035.
The reference program's roundings to bfloat16 on the way count: a program that leaves them out, or rounds other values in their place, can miss the bound.
Values may be sent and summed in bfloat16 or wider, within the bound.
No kernel may reach another device: no remote copies, remote signals or barrier semaphores. Data moves between devices by JAX's collectives and lax.ppermute only.
A program may use at most 128 MiB of HBM per device.

```python
import math
import jax
import jax.numpy as jnp
import numpy as np
from jax import lax

D_LAT = 512
HEADS = 128
DK = 128
BLK = 64
TOPK = 4
TOK_DEV = 256
TOKENS = 8192
QB = 4
CAP = 2
NBLOCKS = 128
HPG = 32
GROUPS = 4
DOCMAX = 4096
DOCS = 4
N_FSDP = 32


def draw_queries(key, part):
    key_values = jax.random.fold_in(key, 0)
    drawn = jax.random.normal(key_values, (TOKENS, HEADS, DK), jnp.float32)
    return drawn.astype(jnp.bfloat16)


def draw_block_lists(key, part):
    device_count = TOKENS // TOK_DEV
    slot_total = QB * (TOPK - 1)
    key_order, key_base = jax.random.split(key)
    order_scores = jax.random.randint(key_order, (device_count, slot_total), 0, 1 << 16) * slot_total + jnp.arange(slot_total)[None, :]
    sort_order = jnp.argsort(order_scores, axis=1)
    slot_rank = jnp.argsort(sort_order, axis=1)
    distance = 1 + slot_rank // CAP
    device_ids = jnp.arange(device_count)[:, None, None]
    owner_ids = device_ids - distance.reshape(device_count, QB, TOPK - 1)
    base_offset = jax.random.randint(key_base, (device_count, QB, 1), 0, QB)
    column_ids = jnp.arange(1, TOPK)[None, None, :]
    query_ids = jnp.arange(QB)[None, :, None]
    local_far = (base_offset + column_ids) % QB
    local_own = (query_ids + 1 + (base_offset + column_ids) % (QB - 1)) % QB
    chosen = jnp.where(owner_ids < 0, device_ids * QB + local_own, owner_ids * QB + local_far)
    own_column = device_ids * QB + query_ids
    return jnp.concatenate([own_column, chosen], axis=2).reshape(NBLOCKS, TOPK).astype(jnp.int32)


def shard_levels(stream_key, shape, shards, smallest, top_value):
    factor_of = 1.0
    for dim, shards_of in shards:
        steps = jax.random.uniform(jax.random.fold_in(jax.random.fold_in(stream_key, 6), dim), (shards_of,), jnp.float32, smallest / len(shards), top_value / len(shards))
        factor_of = factor_of * jnp.repeat(jnp.exp(steps), shape[dim] // shards_of).reshape((-1,) + (1,) * (len(shape) - 1 - dim))
    return factor_of


def length_profile(number_of, total, bound, slope):
    portions = [(1 << 20) // math.isqrt(grade ** slope) + 1 for grade in range(2, number_of + 1)]
    rest, given = total - bound - (number_of - 1), [1] * (number_of - 1)
    while rest > 0:
        movable = [i for i in range(number_of - 1) if given[i] < bound]
        whole, budget = sum([portions[i] for i in movable]), rest
        for i in movable:
            addition = min(bound - given[i], max(1, budget * portions[i] // whole), rest)
            given[i] = given[i] + addition
            rest = rest - addition
    return np.array([bound] + given)


def ragged_sizes(rng, count, total, bound, slope):
    if count == 2:
        one = jax.random.randint(rng, (), max(1, total - bound), min(bound, total - 1) + 1)
        return jnp.stack([one, total - one])
    lengths = jnp.asarray(length_profile(count, total, bound, slope), jnp.int32)
    twos = (count - 1) // 2
    source_of, receiver = lengths[1:1 + 2 * twos:2], lengths[2:2 + 2 * twos:2]
    room = jnp.minimum(source_of - 1, bound - receiver)
    moved = jax.random.randint(jax.random.fold_in(rng, 1), (twos,), 0, 1 << 20) % (room + 1)
    lengths = lengths.at[1:1 + 2 * twos:2].set(source_of - moved).at[2:2 + 2 * twos:2].set(receiver + moved)
    return lengths[jax.random.permutation(jax.random.fold_in(rng, 2), count)]


def gaussian(own_key, dims, scale, bound, pieces=(), kind=jnp.bfloat16):
    loudness = shard_levels(own_key, dims, pieces, -0.22, 0.18) if pieces else 1.0
    values = jax.random.normal(own_key, dims, jnp.float32) * scale * loudness
    return jnp.minimum(jnp.maximum(values, -bound), bound).astype(kind)


def setup_inputs(seed: int = 0) -> dict:
    streams_of = jax.random.split(jax.random.key(seed), 7)
    latents = gaussian(streams_of[0], (TOKENS, D_LAT), 1.0, 6.0, ((0, 32),))
    queries = draw_queries(jax.random.fold_in(streams_of[6], 71), 0)
    grad_out = gaussian(streams_of[2], (TOKENS, HEADS, DK), 1.0, 6.0, ((0, 32), (1, 4)))
    kv_weight = gaussian(streams_of[3], (GROUPS, HPG, D_LAT, 2 * DK), D_LAT ** -0.5, 0.25, ((0, 4), (1, 32)))
    doc_ids = jnp.searchsorted(jnp.cumsum(ragged_sizes(streams_of[4], DOCS, TOKENS, DOCMAX, 2)), jnp.arange(TOKENS), side="right").astype(jnp.int32)
    block_lists = draw_block_lists(jax.random.fold_in(streams_of[6], 71), 0)
    return dict(latents=latents, queries=queries, grad_out=grad_out, kv_weight=kv_weight, doc_ids=doc_ids, block_lists=block_lists)


NEG_FILL = -1e30


def reference(latents, queries, grad_out, kv_weight, doc_ids, block_lists):
    head_weights = kv_weight.reshape(HEADS, D_LAT, 2 * DK)
    offsets = jnp.arange(BLK, dtype=jnp.int32)
    key_pos = (block_lists.astype(jnp.int32)[:, :, None] * BLK + offsets[None, None, :]).reshape(NBLOCKS, TOPK * BLK).astype(jnp.int32)
    query_pos = jnp.arange(TOKENS, dtype=jnp.int32).reshape(NBLOCKS, BLK)
    key_doc = jnp.take(doc_ids, key_pos)
    query_doc = jnp.take(doc_ids, query_pos)
    visible = (key_doc[:, None, :] == query_doc[:, :, None]) & (key_pos[:, None, :] <= query_pos[:, :, None])
    flat_pos = key_pos.reshape(-1)
    score_scale = DK ** -0.5
    run_rows = NBLOCKS * TOPK * BLK // N_FSDP
    slot_lat = jnp.take(latents, flat_pos, axis=0).astype(jnp.float32).reshape(N_FSDP, run_rows, D_LAT)

    def one_head(lat_accum, head_inputs):
        w_head, q_head, g_head = head_inputs
        expanded = jnp.dot(latents, w_head, preferred_element_type=jnp.float32).astype(jnp.bfloat16)
        slot_kv = jnp.take(expanded, flat_pos, axis=0).astype(jnp.float32).reshape(NBLOCKS, TOPK * BLK, 2 * DK)
        key_rows = slot_kv[:, :, :DK]
        value_rows = slot_kv[:, :, DK:]
        q_rows = q_head.astype(jnp.float32).reshape(NBLOCKS, BLK, DK)
        g_rows = g_head.astype(jnp.float32).reshape(NBLOCKS, BLK, DK)
        scores = jnp.einsum("qbd,qkd->qbk", q_rows, key_rows) * score_scale
        scores = jnp.where(visible, scores, NEG_FILL)
        row_max = jnp.max(scores, axis=-1, keepdims=True)
        exp_scores = jnp.exp(scores - row_max)
        softmax_p = exp_scores / jnp.sum(exp_scores, axis=-1, keepdims=True)
        probs_low = lax.optimization_barrier(softmax_p.astype(jnp.bfloat16)).astype(jnp.float32)
        attended = jnp.einsum("qbk,qkd->qbd", probs_low, value_rows)
        delta_rows = jnp.sum(g_rows * attended, axis=-1, keepdims=True)
        grad_probs = jnp.einsum("qbd,qkd->qbk", g_rows, value_rows)
        grad_scores = lax.optimization_barrier((softmax_p * (grad_probs - delta_rows)).astype(jnp.bfloat16)).astype(jnp.float32)
        grad_q = (jnp.einsum("qbk,qkd->qbd", grad_scores, key_rows) * score_scale).astype(jnp.bfloat16)
        grad_k = (jnp.einsum("qbk,qbd->qkd", grad_scores, q_rows) * score_scale).astype(jnp.bfloat16)
        grad_v = jnp.einsum("qbk,qbd->qkd", probs_low, g_rows).astype(jnp.bfloat16)
        grad_kv = lax.optimization_barrier(jnp.concatenate([grad_k, grad_v], axis=-1).reshape(-1, 2 * DK)).astype(jnp.float32)
        token_kv = jnp.zeros((TOKENS, 2 * DK), jnp.float32).at[flat_pos].add(grad_kv)
        lat_accum = lat_accum + lax.dot_general(token_kv, w_head.astype(jnp.float32), (((1,), (1,)), ((), ())), precision=lax.Precision.HIGHEST)
        partial_w = jnp.einsum("grd,grk->gdk", slot_lat, grad_kv.reshape(N_FSDP, run_rows, 2 * DK), precision=lax.Precision.HIGHEST)
        partial_w = lax.optimization_barrier(partial_w.astype(jnp.bfloat16)).astype(jnp.float32)
        return lat_accum, (grad_q.reshape(TOKENS, DK), jnp.sum(partial_w, axis=0))

    lat_start = jnp.zeros((TOKENS, D_LAT), jnp.float32)
    head_inputs = (head_weights, jnp.transpose(queries, (1, 0, 2)), jnp.transpose(grad_out, (1, 0, 2)))
    grad_latents, stacked = lax.scan(one_head, lat_start, head_inputs)
    grad_heads, grad_w_heads = stacked
    grad_queries = jnp.transpose(grad_heads, (1, 0, 2))
    grad_weight = grad_w_heads.reshape(GROUPS, HPG, D_LAT, 2 * DK)
    return (grad_queries, grad_latents, grad_weight)
```

```python
import jax
import jax.numpy as jnp
from jax import lax
from jax.sharding import PartitionSpec as P

BLK = 64
TOPK = 4
DIST = 6


NEG_FILL = -1e30


def passed_along(block, axis, distance):
    devices = range(lax.axis_size(axis))
    route = [(i - distance, i) for i in devices if i - distance in devices]
    return lax.ppermute(block, axis, route)


def all_heads(w_all, queries, grad_out, key_lat, visible, score_scale, block_count):
    tok_rows, head_count, head_dim = queries.shape
    expanded = jnp.einsum(
        "sl,hlc->hsc", key_lat, w_all, preferred_element_type=jnp.float32
    ).astype(jnp.bfloat16)
    expanded = expanded.reshape(head_count, block_count, -1, 2 * head_dim)
    key_rows = expanded[..., :head_dim]
    value_rows = expanded[..., head_dim:]
    q_all = queries.reshape(block_count, BLK, head_count, head_dim)
    g_all = grad_out.reshape(block_count, BLK, head_count, head_dim)
    scores = (
        jnp.einsum("qbhd,hqkd->hqbk", q_all, key_rows, preferred_element_type=jnp.float32)
        * score_scale
    )
    scores = jnp.where(visible[None], scores, NEG_FILL)
    row_max = jnp.max(scores, axis=-1, keepdims=True)
    exp_scores = jnp.exp(scores - row_max)
    softmax_p = exp_scores / jnp.sum(exp_scores, axis=-1, keepdims=True)
    probs_low = softmax_p.astype(jnp.bfloat16)
    attended = jnp.einsum(
        "hqbk,hqkd->hqbd", probs_low, value_rows, preferred_element_type=jnp.float32
    )
    g_t = jnp.transpose(g_all, (2, 0, 1, 3))
    delta_rows = jnp.sum(g_t.astype(jnp.float32) * attended, axis=-1, keepdims=True)
    grad_probs = jnp.einsum(
        "hqbd,hqkd->hqbk", g_t, value_rows, preferred_element_type=jnp.float32
    )
    grad_scores = (softmax_p * (grad_probs - delta_rows)).astype(jnp.bfloat16)
    grad_q = (
        jnp.einsum("hqbk,hqkd->qbhd", grad_scores, key_rows, preferred_element_type=jnp.float32)
        * score_scale
    ).astype(jnp.bfloat16)
    grad_k = (
        jnp.einsum("hqbk,qbhd->hqkd", grad_scores, q_all, preferred_element_type=jnp.float32)
        * score_scale
    ).astype(jnp.bfloat16)
    grad_v = jnp.einsum(
        "hqbk,hqbd->hqkd", probs_low, g_t, preferred_element_type=jnp.float32
    ).astype(jnp.bfloat16)
    grad_kv = jnp.concatenate([grad_k, grad_v], axis=-1).reshape(head_count, -1, 2 * head_dim)
    lat_part = jnp.einsum("hsc,hlc->sl", grad_kv, w_all, preferred_element_type=jnp.float32)
    grad_w = jnp.einsum("sl,hsc->hlc", key_lat, grad_kv, preferred_element_type=jnp.float32)
    return (grad_q.reshape(tok_rows, head_count, head_dim), lat_part, grad_w)


def visibility(doc_ids, list_rows, query_start, block_count):
    offsets = jnp.arange(BLK, dtype=jnp.int32)
    key_pos = (list_rows[:, :, None] * BLK + offsets[None, None, :]).reshape(block_count, -1)
    query_pos = (query_start + jnp.arange(block_count * BLK, dtype=jnp.int32)).reshape(
        block_count, BLK
    )
    key_doc = jnp.take(doc_ids, key_pos)
    query_doc = jnp.take(doc_ids, query_pos)
    visible = (key_doc[:, None, :] == query_doc[:, :, None]) & (
        key_pos[:, None, :] <= query_pos[:, :, None]
    )
    return (key_pos, visible)


def earlier_count(flags):
    positions = jnp.arange(flags.shape[0])
    earlier = positions[None, :] < positions[:, None]
    return jnp.sum(flags & earlier, axis=1)


def slot_ranks(owner_ids):
    positions = jnp.arange(owner_ids.shape[0])
    same_owner = owner_ids[None, :] == owner_ids[:, None]
    earlier = positions[None, :] < positions[:, None]
    return jnp.sum(same_owner & earlier, axis=1)


def per_device(latents, queries, grad_out, kv_weight, doc_ids, block_lists):
    device_pos = lax.axis_index("fsdp")
    tok_rows, lat_width = latents.shape
    head_dim = queries.shape[2]
    head_count = queries.shape[1]
    block_count = tok_rows // BLK
    extra_picks = TOPK - 1
    slot_cap = block_count * extra_picks // DIST
    lat_share = lat_width // lax.axis_size("grp")
    score_scale = head_dim ** (-0.5)
    own_lists = lax.dynamic_slice_in_dim(block_lists, device_pos * block_count, block_count, 0)
    remote_ids = own_lists[:, 1:].reshape(-1)
    owner_ids = remote_ids // block_count
    owner_ranks = slot_ranks(owner_ids)
    remote_pool = jnp.where(
        owner_ids == device_pos,
        remote_ids % block_count,
        block_count + (device_pos - owner_ids - 1) * slot_cap + owner_ranks,
    )
    pool_index = jnp.concatenate(
        [
            jnp.arange(block_count, dtype=jnp.int32)[:, None],
            remote_pool.reshape(block_count, extra_picks),
        ],
        axis=1,
    )
    local_blocks = latents.reshape(block_count, BLK, lat_width)
    send_lists = []
    arrived = []
    for distance in range(1, DIST + 1):
        reader_lists = lax.dynamic_slice_in_dim(
            block_lists, (device_pos + distance) * block_count, block_count, 0
        )
        reader_remote = reader_lists[:, 1:].reshape(-1)
        wanted = reader_remote // block_count == device_pos
        reader_ranks = earlier_count(wanted[None, :] & jnp.ones((wanted.shape[0], 1), bool))
        choose_table = wanted[None, :] & (reader_ranks[None, :] == jnp.arange(slot_cap)[:, None])
        send_index = jnp.sum(
            jnp.where(choose_table, (reader_remote % block_count)[None, :], 0), axis=1
        )
        send_lists.append(send_index)
        outgoing = jnp.take(local_blocks, send_index, axis=0)
        arrived.append(passed_along(outgoing, "fsdp", distance))
    fetched = jnp.concatenate(arrived, axis=0)
    block_pool = jnp.concatenate([local_blocks, fetched], axis=0)
    key_lat = jnp.take(block_pool, pool_index.reshape(-1), axis=0).reshape(-1, lat_width)
    key_pos, visible = visibility(doc_ids, own_lists, device_pos * tok_rows, block_count)

    w_piece = lax.all_gather(kv_weight, "fsdp", axis=1, tiled=True)[0]
    grad_q_all, grad_lat, grad_w_all = all_heads(
        w_piece, queries, grad_out, key_lat, visible, score_scale, block_count
    )
    grad_weight = lax.psum_scatter(
        grad_w_all.astype(jnp.bfloat16), "fsdp", scatter_dimension=0, tiled=True
    ).astype(jnp.float32)[None]
    slot_grads = grad_lat.reshape(block_count, TOPK, BLK, lat_width)
    lat_shares = lax.psum_scatter(slot_grads, "grp", scatter_dimension=3, tiled=True).reshape(
        block_count * TOPK, BLK * lat_share
    )
    flat_pool = pool_index.reshape(-1)
    own_table = (flat_pool[None, :] == jnp.arange(block_count)[:, None]).astype(jnp.float32)
    lat_total = jnp.dot(own_table, lat_shares, precision=lax.Precision.HIGHEST)
    for distance in range(1, DIST + 1):
        slot_ids = block_count + (distance - 1) * slot_cap + jnp.arange(slot_cap)
        pick_table = (flat_pool[None, :] == slot_ids[:, None]).astype(jnp.float32)
        outgoing = jnp.dot(pick_table, lat_shares, precision=lax.Precision.HIGHEST)
        returned = passed_along(outgoing, "fsdp", -distance)
        place_table = (
            send_lists[distance - 1][None, :] == jnp.arange(block_count)[:, None]
        ).astype(jnp.float32)
        lat_total = lat_total + jnp.dot(place_table, returned, precision=lax.Precision.HIGHEST)
    grad_latents = lat_total.reshape(tok_rows, lat_share)
    return (grad_q_all, grad_latents, grad_weight)


def solution(mesh):
    return jax.shard_map(
        per_device,
        mesh=mesh,
        in_specs=(
            P("fsdp", None),
            P("fsdp", "grp", None),
            P("fsdp", "grp", None),
            P("grp", "fsdp", None, None),
            P(),
            P(),
        ),
        out_specs=(P("fsdp", "grp", None), P("fsdp", "grp"), P("grp", "fsdp", None, None)),
        check_vma=False,
    )
```

```python
import jax
import jax.numpy as jnp
from jax import lax
from jax.sharding import PartitionSpec as P

BLK = 64
TOPK = 4
DIST = 6


NEG_FILL = -1e30


def passed_along(block, axis, distance):
    devices = range(lax.axis_size(axis))
    route = [(i - distance, i) for i in devices if i - distance in devices]
    return lax.ppermute(block, axis, route)


def all_heads(w_all, queries, grad_out, key_lat, visible, score_scale, block_count):
    tok_rows, head_count, head_dim = queries.shape
    expanded = jnp.einsum(
        "sl,hlc->hsc", key_lat, w_all, preferred_element_type=jnp.float32
    ).astype(jnp.bfloat16)
    expanded = expanded.reshape(head_count, block_count, -1, 2 * head_dim)
    key_rows = expanded[..., :head_dim]
    value_rows = expanded[..., head_dim:]
    q_all = queries.reshape(block_count, BLK, head_count, head_dim)
    g_all = grad_out.reshape(block_count, BLK, head_count, head_dim)
    scores = (
        jnp.einsum("qbhd,hqkd->hqbk", q_all, key_rows, preferred_element_type=jnp.float32)
        * score_scale
    )
    scores = jnp.where(visible[None], scores, NEG_FILL)
    row_max = jnp.max(scores, axis=-1, keepdims=True)
    exp_scores = jnp.exp(scores - row_max)
    softmax_p = exp_scores / jnp.sum(exp_scores, axis=-1, keepdims=True)
    probs_low = softmax_p.astype(jnp.bfloat16)
    attended = jnp.einsum(
        "hqbk,hqkd->hqbd", probs_low, value_rows, preferred_element_type=jnp.float32
    )
    g_t = jnp.transpose(g_all, (2, 0, 1, 3))
    delta_rows = jnp.sum(g_t.astype(jnp.float32) * attended, axis=-1, keepdims=True)
    grad_probs = jnp.einsum(
        "hqbd,hqkd->hqbk", g_t, value_rows, preferred_element_type=jnp.float32
    )
    grad_scores = (softmax_p * (grad_probs - delta_rows)).astype(jnp.bfloat16)
    grad_q = (
        jnp.einsum("hqbk,hqkd->qbhd", grad_scores, key_rows, preferred_element_type=jnp.float32)
        * score_scale
    ).astype(jnp.bfloat16)
    grad_k = (
        jnp.einsum("hqbk,qbhd->hqkd", grad_scores, q_all, preferred_element_type=jnp.float32)
        * score_scale
    ).astype(jnp.bfloat16)
    grad_v = jnp.einsum(
        "hqbk,hqbd->hqkd", probs_low, g_t, preferred_element_type=jnp.float32
    ).astype(jnp.bfloat16)
    grad_kv = jnp.concatenate([grad_k, grad_v], axis=-1).reshape(head_count, -1, 2 * head_dim)
    lat_part = jnp.einsum("hsc,hlc->sl", grad_kv, w_all, preferred_element_type=jnp.float32)
    grad_w = jnp.einsum("sl,hsc->hlc", key_lat, grad_kv, preferred_element_type=jnp.float32)
    return (grad_q.reshape(tok_rows, head_count, head_dim), lat_part, grad_w)


def visibility(doc_ids, list_rows, query_start, block_count):
    offsets = jnp.arange(BLK, dtype=jnp.int32)
    key_pos = (list_rows[:, :, None] * BLK + offsets[None, None, :]).reshape(block_count, -1)
    query_pos = (query_start + jnp.arange(block_count * BLK, dtype=jnp.int32)).reshape(
        block_count, BLK
    )
    key_doc = jnp.take(doc_ids, key_pos)
    query_doc = jnp.take(doc_ids, query_pos)
    visible = (key_doc[:, None, :] == query_doc[:, :, None]) & (
        key_pos[:, None, :] <= query_pos[:, :, None]
    )
    return (key_pos, visible)


def earlier_count(flags):
    positions = jnp.arange(flags.shape[0])
    earlier = positions[None, :] < positions[:, None]
    return jnp.sum(flags & earlier, axis=1)


def slot_ranks(owner_ids):
    positions = jnp.arange(owner_ids.shape[0])
    same_owner = owner_ids[None, :] == owner_ids[:, None]
    earlier = positions[None, :] < positions[:, None]
    return jnp.sum(same_owner & earlier, axis=1)


def per_device(latents, queries, grad_out, kv_weight, doc_ids, block_lists):
    device_pos = lax.axis_index("fsdp")
    tok_rows, lat_width = latents.shape
    head_dim = queries.shape[2]
    head_count = queries.shape[1]
    block_count = tok_rows // BLK
    extra_picks = TOPK - 1
    slot_cap = block_count * extra_picks // DIST
    lat_share = lat_width // lax.axis_size("grp")
    score_scale = head_dim ** (-0.5)
    own_lists = lax.dynamic_slice_in_dim(block_lists, device_pos * block_count, block_count, 0)
    remote_ids = own_lists[:, 1:].reshape(-1)
    owner_ids = remote_ids // block_count
    owner_ranks = slot_ranks(owner_ids)
    remote_pool = jnp.where(
        owner_ids == device_pos,
        remote_ids % block_count,
        block_count + (device_pos - owner_ids - 1) * slot_cap + owner_ranks,
    )
    pool_index = jnp.concatenate(
        [
            jnp.arange(block_count, dtype=jnp.int32)[:, None],
            remote_pool.reshape(block_count, extra_picks),
        ],
        axis=1,
    )
    local_blocks = latents.reshape(block_count, BLK, lat_width)
    send_lists = []
    arrived = []
    for distance in range(1, DIST + 1):
        reader_lists = lax.dynamic_slice_in_dim(
            block_lists, (device_pos + distance) * block_count, block_count, 0
        )
        reader_remote = reader_lists[:, 1:].reshape(-1)
        wanted = reader_remote // block_count == device_pos
        reader_ranks = earlier_count(wanted[None, :] & jnp.ones((wanted.shape[0], 1), bool))
        choose_table = wanted[None, :] & (reader_ranks[None, :] == jnp.arange(slot_cap)[:, None])
        send_index = jnp.sum(
            jnp.where(choose_table, (reader_remote % block_count)[None, :], 0), axis=1
        )
        send_lists.append(send_index)
        outgoing = jnp.take(local_blocks, send_index, axis=0)
        arrived.append(passed_along(outgoing, "fsdp", distance))
    fetched = jnp.concatenate(arrived, axis=0)
    block_pool = jnp.concatenate([local_blocks, fetched], axis=0)
    key_lat = jnp.take(block_pool, pool_index.reshape(-1), axis=0).reshape(-1, lat_width)
    key_pos, visible = visibility(doc_ids, own_lists, device_pos * tok_rows, block_count)

    fsdp_size = lax.axis_size("fsdp")
    w_copies = jnp.broadcast_to(kv_weight[0], (fsdp_size,) + kv_weight.shape[2:])
    w_piece = lax.all_to_all(w_copies, "fsdp", 0, 0, tiled=True)
    grad_q_all, grad_lat, grad_w_all = all_heads(
        w_piece, queries, grad_out, key_lat, visible, score_scale, block_count
    )
    run_partials = lax.all_to_all(grad_w_all.astype(jnp.bfloat16), "fsdp", 0, 0, tiled=True)
    grad_weight = jnp.sum(run_partials.astype(jnp.float32), axis=0, keepdims=True)[None]
    slot_grads = grad_lat.reshape(block_count, TOPK, BLK, lat_width)
    lat_shares = lax.psum_scatter(slot_grads, "grp", scatter_dimension=3, tiled=True).reshape(
        block_count * TOPK, BLK * lat_share
    )
    flat_pool = pool_index.reshape(-1)
    own_table = (flat_pool[None, :] == jnp.arange(block_count)[:, None]).astype(jnp.float32)
    lat_total = jnp.dot(own_table, lat_shares, precision=lax.Precision.HIGHEST)
    for distance in range(1, DIST + 1):
        slot_ids = block_count + (distance - 1) * slot_cap + jnp.arange(slot_cap)
        pick_table = (flat_pool[None, :] == slot_ids[:, None]).astype(jnp.float32)
        outgoing = jnp.dot(pick_table, lat_shares, precision=lax.Precision.HIGHEST)
        returned = passed_along(outgoing, "fsdp", -distance)
        place_table = (
            send_lists[distance - 1][None, :] == jnp.arange(block_count)[:, None]
        ).astype(jnp.float32)
        lat_total = lat_total + jnp.dot(place_table, returned, precision=lax.Precision.HIGHEST)
    grad_latents = lat_total.reshape(tok_rows, lat_share)
    return (grad_q_all, grad_latents, grad_weight)


def solution(mesh):
    return jax.shard_map(
        per_device,
        mesh=mesh,
        in_specs=(
            P("fsdp", None),
            P("fsdp", "grp", None),
            P("fsdp", "grp", None),
            P("grp", "fsdp", None, None),
            P(),
            P(),
        ),
        out_specs=(P("fsdp", "grp", None), P("fsdp", "grp"), P("grp", "fsdp", None, None)),
        check_vma=False,
    )
```

```python
import jax
import jax.numpy as jnp
from jax import lax
from jax.sharding import PartitionSpec as P

BLK = 64
TOPK = 4
DIST = 6


NEG_FILL = -1e30


def passed_along(block, axis, distance):
    devices = range(lax.axis_size(axis))
    route = [(i - distance, i) for i in devices if i - distance in devices]
    return lax.ppermute(block, axis, route)


def all_heads(w_keys, w_values, queries, grad_out, key_lat, visible, score_scale, block_count):
    tok_rows, head_count, head_dim = queries.shape

    def expand(w_part):
        rows = jnp.einsum("sl,hlc->hsc", key_lat, w_part, preferred_element_type=jnp.float32)
        return rows.astype(jnp.bfloat16).reshape(head_count, block_count, -1, head_dim)

    def weight_grad(grad_part):
        return jnp.einsum(
            "sl,hsc->hlc", key_lat, grad_part, preferred_element_type=jnp.float32
        ).astype(jnp.bfloat16)

    key_rows = expand(w_keys)
    value_rows = expand(w_values)
    q_all = queries.reshape(block_count, BLK, head_count, head_dim)
    g_all = grad_out.reshape(block_count, BLK, head_count, head_dim)
    scores = (
        jnp.einsum("qbhd,hqkd->hqbk", q_all, key_rows, preferred_element_type=jnp.float32)
        * score_scale
    )
    scores = jnp.where(visible[None], scores, NEG_FILL)
    row_max = jnp.max(scores, axis=-1, keepdims=True)
    exp_scores = jnp.exp(scores - row_max)
    softmax_p = exp_scores / jnp.sum(exp_scores, axis=-1, keepdims=True)
    probs_low = softmax_p.astype(jnp.bfloat16)
    g_t = jnp.transpose(g_all, (2, 0, 1, 3))
    grad_v = jnp.einsum(
        "hqbk,hqbd->hqkd", probs_low, g_t, preferred_element_type=jnp.float32
    ).astype(jnp.bfloat16).reshape(head_count, -1, head_dim)
    grad_w_values = weight_grad(grad_v)
    attended = jnp.einsum(
        "hqbk,hqkd->hqbd", probs_low, value_rows, preferred_element_type=jnp.float32
    )
    delta_rows = jnp.sum(g_t.astype(jnp.float32) * attended, axis=-1, keepdims=True)
    grad_probs = jnp.einsum(
        "hqbd,hqkd->hqbk", g_t, value_rows, preferred_element_type=jnp.float32
    )
    grad_scores = (softmax_p * (grad_probs - delta_rows)).astype(jnp.bfloat16)
    grad_q = (
        jnp.einsum("hqbk,hqkd->qbhd", grad_scores, key_rows, preferred_element_type=jnp.float32)
        * score_scale
    ).astype(jnp.bfloat16)
    grad_k = (
        jnp.einsum("hqbk,qbhd->hqkd", grad_scores, q_all, preferred_element_type=jnp.float32)
        * score_scale
    ).astype(jnp.bfloat16).reshape(head_count, -1, head_dim)
    lat_part = jnp.einsum(
        "hsc,hlc->sl", grad_k, w_keys, preferred_element_type=jnp.float32
    ) + jnp.einsum("hsc,hlc->sl", grad_v, w_values, preferred_element_type=jnp.float32)
    grad_w_keys = weight_grad(grad_k)
    return (grad_q.reshape(tok_rows, head_count, head_dim), lat_part, grad_w_keys, grad_w_values)


def visibility(doc_ids, list_rows, query_start, block_count):
    offsets = jnp.arange(BLK, dtype=jnp.int32)
    key_pos = (list_rows[:, :, None] * BLK + offsets[None, None, :]).reshape(block_count, -1)
    query_pos = (query_start + jnp.arange(block_count * BLK, dtype=jnp.int32)).reshape(
        block_count, BLK
    )
    key_doc = jnp.take(doc_ids, key_pos)
    query_doc = jnp.take(doc_ids, query_pos)
    visible = (key_doc[:, None, :] == query_doc[:, :, None]) & (
        key_pos[:, None, :] <= query_pos[:, :, None]
    )
    return (key_pos, visible)


def earlier_count(flags):
    positions = jnp.arange(flags.shape[0])
    earlier = positions[None, :] < positions[:, None]
    return jnp.sum(flags & earlier, axis=1)


def slot_ranks(owner_ids):
    positions = jnp.arange(owner_ids.shape[0])
    same_owner = owner_ids[None, :] == owner_ids[:, None]
    earlier = positions[None, :] < positions[:, None]
    return jnp.sum(same_owner & earlier, axis=1)


def per_device(latents, queries, grad_out, kv_weight, doc_ids, block_lists):
    device_pos = lax.axis_index("fsdp")
    tok_rows, lat_width = latents.shape
    head_dim = queries.shape[2]
    head_count = queries.shape[1]
    block_count = tok_rows // BLK
    extra_picks = TOPK - 1
    slot_cap = block_count * extra_picks // DIST
    lat_share = lat_width // lax.axis_size("grp")
    score_scale = head_dim ** (-0.5)
    own_lists = lax.dynamic_slice_in_dim(block_lists, device_pos * block_count, block_count, 0)
    remote_ids = own_lists[:, 1:].reshape(-1)
    owner_ids = remote_ids // block_count
    owner_ranks = slot_ranks(owner_ids)
    remote_pool = jnp.where(
        owner_ids == device_pos,
        remote_ids % block_count,
        block_count + (device_pos - owner_ids - 1) * slot_cap + owner_ranks,
    )
    pool_index = jnp.concatenate(
        [
            jnp.arange(block_count, dtype=jnp.int32)[:, None],
            remote_pool.reshape(block_count, extra_picks),
        ],
        axis=1,
    )
    local_blocks = latents.reshape(block_count, BLK, lat_width)
    send_lists = []
    arrived = []
    for distance in range(1, DIST + 1):
        reader_lists = lax.dynamic_slice_in_dim(
            block_lists, (device_pos + distance) * block_count, block_count, 0
        )
        reader_remote = reader_lists[:, 1:].reshape(-1)
        wanted = reader_remote // block_count == device_pos
        reader_ranks = earlier_count(wanted[None, :] & jnp.ones((wanted.shape[0], 1), bool))
        choose_table = wanted[None, :] & (reader_ranks[None, :] == jnp.arange(slot_cap)[:, None])
        send_index = jnp.sum(
            jnp.where(choose_table, (reader_remote % block_count)[None, :], 0), axis=1
        )
        send_lists.append(send_index)
        outgoing = jnp.take(local_blocks, send_index, axis=0)
        arrived.append(passed_along(outgoing, "fsdp", distance))
    fetched = jnp.concatenate(arrived, axis=0)
    block_pool = jnp.concatenate([local_blocks, fetched], axis=0)
    key_lat = jnp.take(block_pool, pool_index.reshape(-1), axis=0).reshape(-1, lat_width)
    key_pos, visible = visibility(doc_ids, own_lists, device_pos * tok_rows, block_count)

    fsdp_size = lax.axis_size("fsdp")

    def gather_heads(w_part):
        copies = jnp.broadcast_to(w_part, (fsdp_size,) + w_part.shape)
        return lax.all_to_all(copies, "fsdp", 0, 0, tiled=True)

    def reduce_runs(partials):
        per_run = lax.all_to_all(partials, "fsdp", 0, 0, tiled=True)
        return jnp.sum(per_run.astype(jnp.float32), axis=0)

    w_keys = gather_heads(kv_weight[0, 0, :, :head_dim])
    w_values = gather_heads(kv_weight[0, 0, :, head_dim:])
    grad_q_all, grad_lat, grad_w_keys, grad_w_values = all_heads(
        w_keys, w_values, queries, grad_out, key_lat, visible, score_scale, block_count
    )
    grad_weight = jnp.concatenate(
        [reduce_runs(grad_w_keys), reduce_runs(grad_w_values)], axis=-1
    )[None, None]
    grp_size = lax.axis_size("grp")
    lat_pieces = jnp.moveaxis(grad_lat.reshape(-1, grp_size, lat_share), 1, 0)
    lat_pieces = lax.all_to_all(lat_pieces, "grp", 0, 0, tiled=True)
    lat_shares = jnp.sum(lat_pieces, axis=0).reshape(block_count * TOPK, BLK * lat_share)
    flat_pool = pool_index.reshape(-1)
    own_table = (flat_pool[None, :] == jnp.arange(block_count)[:, None]).astype(jnp.float32)
    lat_total = jnp.dot(own_table, lat_shares, precision=lax.Precision.HIGHEST)
    for distance in range(1, DIST + 1):
        slot_ids = block_count + (distance - 1) * slot_cap + jnp.arange(slot_cap)
        pick_table = (flat_pool[None, :] == slot_ids[:, None]).astype(jnp.float32)
        outgoing = jnp.dot(pick_table, lat_shares, precision=lax.Precision.HIGHEST)
        returned = passed_along(outgoing, "fsdp", -distance)
        place_table = (
            send_lists[distance - 1][None, :] == jnp.arange(block_count)[:, None]
        ).astype(jnp.float32)
        lat_total = lat_total + jnp.dot(place_table, returned, precision=lax.Precision.HIGHEST)
    grad_latents = lat_total.reshape(tok_rows, lat_share)
    return (grad_q_all, grad_latents, grad_weight)


def solution(mesh):
    return jax.shard_map(
        per_device,
        mesh=mesh,
        in_specs=(
            P("fsdp", None),
            P("fsdp", "grp", None),
            P("fsdp", "grp", None),
            P("grp", "fsdp", None, None),
            P(),
            P(),
        ),
        out_specs=(P("fsdp", "grp", None), P("fsdp", "grp"), P("grp", "fsdp", None, None)),
        check_vma=False,
    )
```

```python
import jax
import jax.numpy as jnp
from jax import lax
from jax.sharding import PartitionSpec as P

BLK = 64
TOPK = 4
DIST = 6


NEG_FILL = -1e30


def passed_along(block, axis, distance):
    devices = range(lax.axis_size(axis))
    route = [(i - distance, i) for i in devices if i - distance in devices]
    return lax.ppermute(block, axis, route)


def all_heads(w_keys, w_values, queries, grad_out, key_lat, visible, score_scale, block_count):
    tok_rows, head_count, head_dim = queries.shape

    def expand(w_part):
        rows = jnp.einsum("sl,hlc->hsc", key_lat, w_part, preferred_element_type=jnp.float32)
        return rows.astype(jnp.bfloat16).reshape(head_count, block_count, -1, head_dim)

    def weight_grad(grad_part):
        return jnp.einsum(
            "sl,hsc->hlc", key_lat, grad_part, preferred_element_type=jnp.float32
        ).astype(jnp.bfloat16)

    key_rows = expand(w_keys)
    value_rows = expand(w_values)
    q_all = queries.reshape(block_count, BLK, head_count, head_dim)
    g_all = grad_out.reshape(block_count, BLK, head_count, head_dim)
    scores = (
        jnp.einsum("qbhd,hqkd->hqbk", q_all, key_rows, preferred_element_type=jnp.float32)
        * score_scale
    )
    scores = jnp.where(visible[None], scores, NEG_FILL)
    row_max = jnp.max(scores, axis=-1, keepdims=True)
    exp_scores = jnp.exp(scores - row_max)
    softmax_p = exp_scores / jnp.sum(exp_scores, axis=-1, keepdims=True)
    probs_low = softmax_p.astype(jnp.bfloat16)
    g_t = jnp.transpose(g_all, (2, 0, 1, 3))
    probs_low, value_rows = lax.optimization_barrier((probs_low, value_rows))
    grad_v = jnp.einsum(
        "hqbk,hqbd->hqkd", probs_low, g_t, preferred_element_type=jnp.float32
    ).astype(jnp.bfloat16).reshape(head_count, -1, head_dim)
    grad_w_values = weight_grad(grad_v)
    return grad_w_values, *score_grads(
        probs_low, softmax_p, g_t, q_all, key_rows, value_rows, w_keys, w_values,
        grad_v, score_scale, weight_grad, tok_rows
    )


def score_grads(probs_low, softmax_p, g_t, q_all, key_rows, value_rows, w_keys, w_values,
                grad_v, score_scale, weight_grad, tok_rows):
    head_count = key_rows.shape[0]
    head_dim = key_rows.shape[-1]
    attended = jnp.einsum(
        "hqbk,hqkd->hqbd", probs_low, value_rows, preferred_element_type=jnp.float32
    )
    delta_rows = jnp.sum(g_t.astype(jnp.float32) * attended, axis=-1, keepdims=True)
    grad_probs = jnp.einsum(
        "hqbd,hqkd->hqbk", g_t, value_rows, preferred_element_type=jnp.float32
    )
    grad_scores = (softmax_p * (grad_probs - delta_rows)).astype(jnp.bfloat16)
    grad_q = (
        jnp.einsum("hqbk,hqkd->qbhd", grad_scores, key_rows, preferred_element_type=jnp.float32)
        * score_scale
    ).astype(jnp.bfloat16)
    grad_k = (
        jnp.einsum("hqbk,qbhd->hqkd", grad_scores, q_all, preferred_element_type=jnp.float32)
        * score_scale
    ).astype(jnp.bfloat16).reshape(head_count, -1, head_dim)
    lat_part = jnp.einsum(
        "hsc,hlc->sl", grad_k, w_keys, preferred_element_type=jnp.float32
    ) + jnp.einsum("hsc,hlc->sl", grad_v, w_values, preferred_element_type=jnp.float32)
    grad_w_keys = weight_grad(grad_k)
    return (grad_q.reshape(tok_rows, head_count, head_dim), lat_part, grad_w_keys)


def visibility(doc_ids, list_rows, query_start, block_count):
    offsets = jnp.arange(BLK, dtype=jnp.int32)
    key_pos = (list_rows[:, :, None] * BLK + offsets[None, None, :]).reshape(block_count, -1)
    query_pos = (query_start + jnp.arange(block_count * BLK, dtype=jnp.int32)).reshape(
        block_count, BLK
    )
    key_doc = jnp.take(doc_ids, key_pos)
    query_doc = jnp.take(doc_ids, query_pos)
    visible = (key_doc[:, None, :] == query_doc[:, :, None]) & (
        key_pos[:, None, :] <= query_pos[:, :, None]
    )
    return (key_pos, visible)


def earlier_count(flags):
    positions = jnp.arange(flags.shape[0])
    earlier = positions[None, :] < positions[:, None]
    return jnp.sum(flags & earlier, axis=1)


def slot_ranks(owner_ids):
    positions = jnp.arange(owner_ids.shape[0])
    same_owner = owner_ids[None, :] == owner_ids[:, None]
    earlier = positions[None, :] < positions[:, None]
    return jnp.sum(same_owner & earlier, axis=1)


def per_device(latents, queries, grad_out, kv_weight, doc_ids, block_lists):
    device_pos = lax.axis_index("fsdp")
    tok_rows, lat_width = latents.shape
    head_dim = queries.shape[2]
    block_count = tok_rows // BLK
    extra_picks = TOPK - 1
    slot_cap = block_count * extra_picks // DIST
    lat_share = lat_width // lax.axis_size("grp")
    score_scale = head_dim ** (-0.5)
    own_lists = lax.dynamic_slice_in_dim(block_lists, device_pos * block_count, block_count, 0)
    remote_ids = own_lists[:, 1:].reshape(-1)
    owner_ids = remote_ids // block_count
    owner_ranks = slot_ranks(owner_ids)
    remote_pool = jnp.where(
        owner_ids == device_pos,
        remote_ids % block_count,
        block_count + (device_pos - owner_ids - 1) * slot_cap + owner_ranks,
    )
    pool_index = jnp.concatenate(
        [
            jnp.arange(block_count, dtype=jnp.int32)[:, None],
            remote_pool.reshape(block_count, extra_picks),
        ],
        axis=1,
    )
    local_blocks = latents.reshape(block_count, BLK, lat_width)
    send_lists = []
    arrived = []
    for distance in range(1, DIST + 1):
        reader_lists = lax.dynamic_slice_in_dim(
            block_lists, (device_pos + distance) * block_count, block_count, 0
        )
        reader_remote = reader_lists[:, 1:].reshape(-1)
        wanted = reader_remote // block_count == device_pos
        reader_ranks = earlier_count(wanted[None, :] & jnp.ones((wanted.shape[0], 1), bool))
        choose_table = wanted[None, :] & (reader_ranks[None, :] == jnp.arange(slot_cap)[:, None])
        send_index = jnp.sum(
            jnp.where(choose_table, (reader_remote % block_count)[None, :], 0), axis=1
        )
        send_lists.append(send_index)
        outgoing = jnp.take(local_blocks, send_index, axis=0)
        arrived.append(passed_along(outgoing, "fsdp", distance))
    fetched = jnp.concatenate(arrived, axis=0)
    block_pool = jnp.concatenate([local_blocks, fetched], axis=0)
    key_lat = jnp.take(block_pool, pool_index.reshape(-1), axis=0).reshape(-1, lat_width)
    _, visible = visibility(doc_ids, own_lists, device_pos * tok_rows, block_count)

    fsdp_size = lax.axis_size("fsdp")

    def gather_heads(w_part):
        copies = jnp.broadcast_to(w_part, (fsdp_size,) + w_part.shape)
        return lax.all_to_all(copies, "fsdp", 0, 0, tiled=True)

    def reduce_runs(partials):
        per_run = lax.all_to_all(partials, "fsdp", 0, 0, tiled=True)
        return jnp.sum(per_run.astype(jnp.float32), axis=0)

    w_keys = gather_heads(kv_weight[0, 0, :, :head_dim])
    w_values = gather_heads(kv_weight[0, 0, :, head_dim:])
    grad_w_values, grad_q_all, grad_lat, grad_w_keys = all_heads(
        w_keys, w_values, queries, grad_out, key_lat, visible, score_scale, block_count
    )
    value_part = reduce_runs(grad_w_values)
    key_part = reduce_runs(grad_w_keys)
    grad_weight = jnp.concatenate([key_part, value_part], axis=-1)[None, None]
    grp_size = lax.axis_size("grp")
    lat_pieces = jnp.moveaxis(grad_lat.reshape(-1, grp_size, lat_share), 1, 0)
    lat_pieces = lax.all_to_all(lat_pieces, "grp", 0, 0, tiled=True)
    lat_shares = jnp.sum(lat_pieces, axis=0).reshape(block_count * TOPK, BLK * lat_share)
    flat_pool = pool_index.reshape(-1)
    own_table = (flat_pool[None, :] == jnp.arange(block_count)[:, None]).astype(jnp.float32)
    lat_total = jnp.dot(own_table, lat_shares, precision=lax.Precision.HIGHEST)
    for distance in range(1, DIST + 1):
        slot_ids = block_count + (distance - 1) * slot_cap + jnp.arange(slot_cap)
        pick_table = (flat_pool[None, :] == slot_ids[:, None]).astype(jnp.float32)
        outgoing = jnp.dot(pick_table, lat_shares, precision=lax.Precision.HIGHEST)
        returned = passed_along(outgoing, "fsdp", -distance)
        place_table = (
            send_lists[distance - 1][None, :] == jnp.arange(block_count)[:, None]
        ).astype(jnp.float32)
        lat_total = lat_total + jnp.dot(place_table, returned, precision=lax.Precision.HIGHEST)
    grad_latents = lat_total.reshape(tok_rows, lat_share)
    return (grad_q_all, grad_latents, grad_weight)


def solution(mesh):
    return jax.shard_map(
        per_device,
        mesh=mesh,
        in_specs=(
            P("fsdp", None),
            P("fsdp", "grp", None),
            P("fsdp", "grp", None),
            P("grp", "fsdp", None, None),
            P(),
            P(),
        ),
        out_specs=(P("fsdp", "grp", None), P("fsdp", "grp"), P("grp", "fsdp", None, None)),
        check_vma=False,
    )
```

```python
import jax
import jax.numpy as jnp
from jax import lax
from jax.sharding import PartitionSpec as P

BLK = 64
TOPK = 4
DIST = 6


NEG_FILL = -1e30


def passed_along(block, axis, distance):
    devices = range(lax.axis_size(axis))
    route = [(i - distance, i) for i in devices if i - distance in devices]
    return lax.ppermute(block, axis, route)


def all_heads(w_keys, w_values, queries, grad_out, key_lat, visible, score_scale, block_count):
    tok_rows, head_count, head_dim = queries.shape

    def expand(w_part):
        rows = jnp.einsum("sl,hlc->hsc", key_lat, w_part, preferred_element_type=jnp.float32)
        return rows.astype(jnp.bfloat16).reshape(head_count, block_count, -1, head_dim)

    def weight_grad(grad_part):
        return jnp.einsum(
            "sl,hsc->hlc", key_lat, grad_part, preferred_element_type=jnp.float32
        ).astype(jnp.bfloat16)

    key_rows = expand(w_keys)
    value_rows = expand(w_values)
    q_all = queries.reshape(block_count, BLK, head_count, head_dim)
    g_all = grad_out.reshape(block_count, BLK, head_count, head_dim)
    scores = (
        jnp.einsum("qbhd,hqkd->hqbk", q_all, key_rows, preferred_element_type=jnp.float32)
        * score_scale
    )
    scores = jnp.where(visible[None], scores, NEG_FILL)
    row_max = jnp.max(scores, axis=-1, keepdims=True)
    exp_scores = jnp.exp(scores - row_max)
    softmax_p = exp_scores / jnp.sum(exp_scores, axis=-1, keepdims=True)
    probs_low = softmax_p.astype(jnp.bfloat16)
    g_t = jnp.transpose(g_all, (2, 0, 1, 3))
    grad_v = jnp.einsum(
        "hqbk,hqbd->hqkd", probs_low, g_t, preferred_element_type=jnp.float32
    ).astype(jnp.bfloat16).reshape(head_count, -1, head_dim)
    grad_w_values = weight_grad(grad_v)
    return grad_w_values, *score_grads(
        probs_low, softmax_p, g_t, q_all, key_rows, value_rows, w_keys, w_values,
        grad_v, score_scale, weight_grad, tok_rows
    )


def score_grads(probs_low, softmax_p, g_t, q_all, key_rows, value_rows, w_keys, w_values,
                grad_v, score_scale, weight_grad, tok_rows):
    head_count = key_rows.shape[0]
    head_dim = key_rows.shape[-1]
    attended = jnp.einsum(
        "hqbk,hqkd->hqbd", probs_low, value_rows, preferred_element_type=jnp.float32
    )
    delta_rows = jnp.sum(g_t.astype(jnp.float32) * attended, axis=-1, keepdims=True)
    grad_probs = jnp.einsum(
        "hqbd,hqkd->hqbk", g_t, value_rows, preferred_element_type=jnp.float32
    )
    grad_scores = (softmax_p * (grad_probs - delta_rows)).astype(jnp.bfloat16)
    grad_q = (
        jnp.einsum("hqbk,hqkd->qbhd", grad_scores, key_rows, preferred_element_type=jnp.float32)
        * score_scale
    ).astype(jnp.bfloat16)
    grad_k = (
        jnp.einsum("hqbk,qbhd->hqkd", grad_scores, q_all, preferred_element_type=jnp.float32)
        * score_scale
    ).astype(jnp.bfloat16).reshape(head_count, -1, head_dim)
    lat_part = jnp.einsum(
        "hsc,hlc->sl", grad_k, w_keys, preferred_element_type=jnp.float32
    ) + jnp.einsum("hsc,hlc->sl", grad_v, w_values, preferred_element_type=jnp.float32)
    grad_w_keys = weight_grad(grad_k)
    return (grad_q.reshape(tok_rows, head_count, head_dim), lat_part, grad_w_keys)


def visibility(doc_ids, list_rows, query_start, block_count):
    offsets = jnp.arange(BLK, dtype=jnp.int32)
    key_pos = (list_rows[:, :, None] * BLK + offsets[None, None, :]).reshape(block_count, -1)
    query_pos = (query_start + jnp.arange(block_count * BLK, dtype=jnp.int32)).reshape(
        block_count, BLK
    )
    key_doc = jnp.take(doc_ids, key_pos)
    query_doc = jnp.take(doc_ids, query_pos)
    visible = (key_doc[:, None, :] == query_doc[:, :, None]) & (
        key_pos[:, None, :] <= query_pos[:, :, None]
    )
    return (key_pos, visible)


def earlier_count(flags):
    positions = jnp.arange(flags.shape[0])
    earlier = positions[None, :] < positions[:, None]
    return jnp.sum(flags & earlier, axis=1)


def slot_ranks(owner_ids):
    positions = jnp.arange(owner_ids.shape[0])
    same_owner = owner_ids[None, :] == owner_ids[:, None]
    earlier = positions[None, :] < positions[:, None]
    return jnp.sum(same_owner & earlier, axis=1)


def per_device(latents, queries, grad_out, kv_weight, doc_ids, block_lists):
    device_pos = lax.axis_index("fsdp")
    tok_rows, lat_width = latents.shape
    head_dim = queries.shape[2]
    block_count = tok_rows // BLK
    extra_picks = TOPK - 1
    slot_cap = block_count * extra_picks // DIST
    lat_share = lat_width // lax.axis_size("grp")
    score_scale = head_dim ** (-0.5)
    own_lists = lax.dynamic_slice_in_dim(block_lists, device_pos * block_count, block_count, 0)
    remote_ids = own_lists[:, 1:].reshape(-1)
    owner_ids = remote_ids // block_count
    owner_ranks = slot_ranks(owner_ids)
    remote_pool = jnp.where(
        owner_ids == device_pos,
        remote_ids % block_count,
        block_count + (device_pos - owner_ids - 1) * slot_cap + owner_ranks,
    )
    pool_index = jnp.concatenate(
        [
            jnp.arange(block_count, dtype=jnp.int32)[:, None],
            remote_pool.reshape(block_count, extra_picks),
        ],
        axis=1,
    )
    local_blocks = latents.reshape(block_count, BLK, lat_width)
    send_lists = []
    arrived = []
    for distance in range(1, DIST + 1):
        reader_lists = lax.dynamic_slice_in_dim(
            block_lists, (device_pos + distance) * block_count, block_count, 0
        )
        reader_remote = reader_lists[:, 1:].reshape(-1)
        wanted = reader_remote // block_count == device_pos
        reader_ranks = earlier_count(wanted[None, :] & jnp.ones((wanted.shape[0], 1), bool))
        choose_table = wanted[None, :] & (reader_ranks[None, :] == jnp.arange(slot_cap)[:, None])
        send_index = jnp.sum(
            jnp.where(choose_table, (reader_remote % block_count)[None, :], 0), axis=1
        )
        send_lists.append(send_index)
        outgoing = jnp.take(local_blocks, send_index, axis=0)
        arrived.append(passed_along(outgoing, "fsdp", distance))
    fetched = jnp.concatenate(arrived, axis=0)
    block_pool = jnp.concatenate([local_blocks, fetched], axis=0)
    key_lat = jnp.take(block_pool, pool_index.reshape(-1), axis=0).reshape(-1, lat_width)
    _, visible = visibility(doc_ids, own_lists, device_pos * tok_rows, block_count)

    fsdp_size = lax.axis_size("fsdp")

    def gather_heads(w_part):
        copies = jnp.broadcast_to(w_part, (fsdp_size,) + w_part.shape)
        return lax.all_to_all(copies, "fsdp", 0, 0, tiled=True)

    def reduce_runs(partials):
        per_run = lax.all_to_all(partials, "fsdp", 0, 0, tiled=True)
        return jnp.sum(per_run.astype(jnp.float32), axis=0)

    w_keys = gather_heads(kv_weight[0, 0, :, :head_dim])
    w_values = gather_heads(kv_weight[0, 0, :, head_dim:])
    grad_w_values, grad_q_all, grad_lat, grad_w_keys = all_heads(
        w_keys, w_values, queries, grad_out, key_lat, visible, score_scale, block_count
    )
    value_part = reduce_runs(grad_w_values)
    key_part = reduce_runs(grad_w_keys)
    grad_weight = jnp.concatenate([key_part, value_part], axis=-1)[None, None]
    slot_grads = grad_lat.reshape(block_count, TOPK, BLK, lat_width)
    lat_shares = lax.psum_scatter(slot_grads, "grp", scatter_dimension=3, tiled=True)
    lat_shares = lat_shares.reshape(block_count * TOPK, BLK * lat_share)
    flat_pool = pool_index.reshape(-1)
    own_table = (flat_pool[None, :] == jnp.arange(block_count)[:, None]).astype(jnp.float32)
    lat_total = jnp.dot(own_table, lat_shares, precision=lax.Precision.HIGHEST)
    for distance in range(1, DIST + 1):
        slot_ids = block_count + (distance - 1) * slot_cap + jnp.arange(slot_cap)
        pick_table = (flat_pool[None, :] == slot_ids[:, None]).astype(jnp.float32)
        outgoing = jnp.dot(pick_table, lat_shares, precision=lax.Precision.HIGHEST)
        returned = passed_along(outgoing, "fsdp", -distance)
        place_table = (
            send_lists[distance - 1][None, :] == jnp.arange(block_count)[:, None]
        ).astype(jnp.float32)
        lat_total = lat_total + jnp.dot(place_table, returned, precision=lax.Precision.HIGHEST)
    grad_latents = lat_total.reshape(tok_rows, lat_share)
    return (grad_q_all, grad_latents, grad_weight)


def solution(mesh):
    return jax.shard_map(
        per_device,
        mesh=mesh,
        in_specs=(
            P("fsdp", None),
            P("fsdp", "grp", None),
            P("fsdp", "grp", None),
            P("grp", "fsdp", None, None),
            P(),
            P(),
        ),
        out_specs=(P("fsdp", "grp", None), P("fsdp", "grp"), P("grp", "fsdp", None, None)),
        check_vma=False,
    )
```

```python
import jax
import jax.numpy as jnp
from jax import lax
from jax.sharding import PartitionSpec as P

BLK = 64
TOPK = 4
DIST = 6


NEG_FILL = -1e30


def passed_along(block, axis, distance):
    devices = range(lax.axis_size(axis))
    route = [(i - distance, i) for i in devices if i - distance in devices]
    return lax.ppermute(block, axis, route)


def all_heads(w_keys, w_values, queries, grad_out, key_lat, visible, score_scale, block_count):
    tok_rows, head_count, head_dim = queries.shape

    def expand(w_part):
        rows = jnp.einsum("sl,hlc->hsc", key_lat, w_part, preferred_element_type=jnp.float32)
        return rows.astype(jnp.bfloat16).reshape(head_count, block_count, -1, head_dim)

    def weight_grad(grad_part):
        return jnp.einsum(
            "sl,hsc->hlc", key_lat, grad_part, preferred_element_type=jnp.float32
        ).astype(jnp.bfloat16)

    key_rows = expand(w_keys)
    value_rows = expand(w_values)
    q_all = queries.reshape(block_count, BLK, head_count, head_dim)
    g_all = grad_out.reshape(block_count, BLK, head_count, head_dim)
    scores = (
        jnp.einsum("qbhd,hqkd->hqbk", q_all, key_rows, preferred_element_type=jnp.float32)
        * score_scale
    )
    scores = jnp.where(visible[None], scores, NEG_FILL)
    row_max = jnp.max(scores, axis=-1, keepdims=True)
    exp_scores = jnp.exp(scores - row_max)
    softmax_p = exp_scores / jnp.sum(exp_scores, axis=-1, keepdims=True)
    probs_low = softmax_p.astype(jnp.bfloat16)
    g_t = jnp.transpose(g_all, (2, 0, 1, 3))
    grad_v = jnp.einsum(
        "hqbk,hqbd->hqkd", probs_low, g_t, preferred_element_type=jnp.float32
    ).astype(jnp.bfloat16).reshape(head_count, -1, head_dim)
    grad_w_values = weight_grad(grad_v)
    return grad_w_values, *score_grads(
        probs_low, softmax_p, g_t, q_all, key_rows, value_rows, w_keys, w_values,
        grad_v, score_scale, weight_grad, tok_rows
    )


def score_grads(probs_low, softmax_p, g_t, q_all, key_rows, value_rows, w_keys, w_values,
                grad_v, score_scale, weight_grad, tok_rows):
    head_count = key_rows.shape[0]
    head_dim = key_rows.shape[-1]
    attended = jnp.einsum(
        "hqbk,hqkd->hqbd", probs_low, value_rows, preferred_element_type=jnp.float32
    )
    delta_rows = jnp.sum(g_t.astype(jnp.float32) * attended, axis=-1, keepdims=True)
    grad_probs = jnp.einsum(
        "hqbd,hqkd->hqbk", g_t, value_rows, preferred_element_type=jnp.float32
    )
    grad_scores = (softmax_p * (grad_probs - delta_rows)).astype(jnp.bfloat16)
    grad_q = (
        jnp.einsum("hqbk,hqkd->qbhd", grad_scores, key_rows, preferred_element_type=jnp.float32)
        * score_scale
    ).astype(jnp.bfloat16)
    grad_k = (
        jnp.einsum("hqbk,qbhd->hqkd", grad_scores, q_all, preferred_element_type=jnp.float32)
        * score_scale
    ).astype(jnp.bfloat16).reshape(head_count, -1, head_dim)
    lat_part = jnp.einsum(
        "hsc,hlc->sl", grad_k, w_keys, preferred_element_type=jnp.float32
    ) + jnp.einsum("hsc,hlc->sl", grad_v, w_values, preferred_element_type=jnp.float32)
    grad_w_keys = weight_grad(grad_k)
    return (grad_q.reshape(tok_rows, head_count, head_dim), lat_part, grad_w_keys)


def visibility(doc_ids, list_rows, query_start, block_count):
    offsets = jnp.arange(BLK, dtype=jnp.int32)
    key_pos = (list_rows[:, :, None] * BLK + offsets[None, None, :]).reshape(block_count, -1)
    query_pos = (query_start + jnp.arange(block_count * BLK, dtype=jnp.int32)).reshape(
        block_count, BLK
    )
    key_doc = jnp.take(doc_ids, key_pos)
    query_doc = jnp.take(doc_ids, query_pos)
    visible = (key_doc[:, None, :] == query_doc[:, :, None]) & (
        key_pos[:, None, :] <= query_pos[:, :, None]
    )
    return (key_pos, visible)


def earlier_count(flags):
    positions = jnp.arange(flags.shape[0])
    earlier = positions[None, :] < positions[:, None]
    return jnp.sum(flags & earlier, axis=1)


def slot_ranks(owner_ids):
    positions = jnp.arange(owner_ids.shape[0])
    same_owner = owner_ids[None, :] == owner_ids[:, None]
    earlier = positions[None, :] < positions[:, None]
    return jnp.sum(same_owner & earlier, axis=1)


def per_device(latents, queries, grad_out, kv_weight, doc_ids, block_lists):
    device_pos = lax.axis_index("fsdp")
    tok_rows, lat_width = latents.shape
    head_dim = queries.shape[2]
    block_count = tok_rows // BLK
    extra_picks = TOPK - 1
    slot_cap = block_count * extra_picks // DIST
    lat_share = lat_width // lax.axis_size("grp")
    score_scale = head_dim ** (-0.5)
    own_lists = lax.dynamic_slice_in_dim(block_lists, device_pos * block_count, block_count, 0)
    remote_ids = own_lists[:, 1:].reshape(-1)
    owner_ids = remote_ids // block_count
    owner_ranks = slot_ranks(owner_ids)
    remote_pool = jnp.where(
        owner_ids == device_pos,
        remote_ids % block_count,
        block_count + (device_pos - owner_ids - 1) * slot_cap + owner_ranks,
    )
    pool_index = jnp.concatenate(
        [
            jnp.arange(block_count, dtype=jnp.int32)[:, None],
            remote_pool.reshape(block_count, extra_picks),
        ],
        axis=1,
    )
    local_blocks = latents.reshape(block_count, BLK, lat_width)
    send_lists = []
    arrived = []
    for distance in range(1, DIST + 1):
        reader_lists = lax.dynamic_slice_in_dim(
            block_lists, (device_pos + distance) * block_count, block_count, 0
        )
        reader_remote = reader_lists[:, 1:].reshape(-1)
        wanted = reader_remote // block_count == device_pos
        reader_ranks = earlier_count(wanted[None, :] & jnp.ones((wanted.shape[0], 1), bool))
        choose_table = wanted[None, :] & (reader_ranks[None, :] == jnp.arange(slot_cap)[:, None])
        send_index = jnp.sum(
            jnp.where(choose_table, (reader_remote % block_count)[None, :], 0), axis=1
        )
        send_lists.append(send_index)
        outgoing = jnp.take(local_blocks, send_index, axis=0)
        arrived.append(passed_along(outgoing, "fsdp", distance))
    fetched = jnp.concatenate(arrived, axis=0)
    block_pool = jnp.concatenate([local_blocks, fetched], axis=0)
    key_lat = jnp.take(block_pool, pool_index.reshape(-1), axis=0).reshape(-1, lat_width)
    _, visible = visibility(doc_ids, own_lists, device_pos * tok_rows, block_count)

    fsdp_size = lax.axis_size("fsdp")

    def gather_heads(w_part):
        copies = jnp.broadcast_to(w_part, (fsdp_size,) + w_part.shape)
        return lax.all_to_all(copies, "fsdp", 0, 0, tiled=True)

    def reduce_runs(partials):
        per_run = lax.all_to_all(partials, "fsdp", 0, 0, tiled=True)
        return jnp.sum(per_run.astype(jnp.float32), axis=0)

    w_keys = gather_heads(kv_weight[0, 0, :, :head_dim])
    w_values = gather_heads(kv_weight[0, 0, :, head_dim:])
    grad_w_values, grad_q_all, grad_lat, grad_w_keys = all_heads(
        w_keys, w_values, queries, grad_out, key_lat, visible, score_scale, block_count
    )
    value_part = reduce_runs(grad_w_values)
    key_part = reduce_runs(grad_w_keys)
    grad_weight = jnp.concatenate([key_part, value_part], axis=-1)[None, None]
    grp_size = lax.axis_size("grp")
    grp_pos = lax.axis_index("grp")
    lat_pieces = grad_lat.reshape(-1, grp_size, lat_share)
    lat_sum = lax.dynamic_index_in_dim(lat_pieces, grp_pos, 1, False)
    for shift in range(1, grp_size):
        piece = lax.dynamic_index_in_dim(lat_pieces, (grp_pos + shift) % grp_size, 1, False)
        route = [(i, (i + shift) % grp_size) for i in range(grp_size)]
        lat_sum = lat_sum + lax.ppermute(piece, "grp", route)
    lat_shares = lat_sum.reshape(block_count * TOPK, BLK * lat_share)
    flat_pool = pool_index.reshape(-1)
    own_table = (flat_pool[None, :] == jnp.arange(block_count)[:, None]).astype(jnp.float32)
    lat_total = jnp.dot(own_table, lat_shares, precision=lax.Precision.HIGHEST)
    for distance in range(1, DIST + 1):
        slot_ids = block_count + (distance - 1) * slot_cap + jnp.arange(slot_cap)
        pick_table = (flat_pool[None, :] == slot_ids[:, None]).astype(jnp.float32)
        outgoing = jnp.dot(pick_table, lat_shares, precision=lax.Precision.HIGHEST)
        returned = passed_along(outgoing, "fsdp", -distance)
        place_table = (
            send_lists[distance - 1][None, :] == jnp.arange(block_count)[:, None]
        ).astype(jnp.float32)
        lat_total = lat_total + jnp.dot(place_table, returned, precision=lax.Precision.HIGHEST)
    grad_latents = lat_total.reshape(tok_rows, lat_share)
    return (grad_q_all, grad_latents, grad_weight)


def solution(mesh):
    return jax.shard_map(
        per_device,
        mesh=mesh,
        in_specs=(
            P("fsdp", None),
            P("fsdp", "grp", None),
            P("fsdp", "grp", None),
            P("grp", "fsdp", None, None),
            P(),
            P(),
        ),
        out_specs=(P("fsdp", "grp", None), P("fsdp", "grp"), P("grp", "fsdp", None, None)),
        check_vma=False,
    )
```
